512 devices in a mesh: ctx: 64 (over z_hi, y, core), head: 8 (over x, z_lo).
Axes of the slice: x: 4, y: 8, z: 8 (z_hi: 4, z_lo: 2; z = z_hi * 2 + z_lo), core: 2. Of those that a mesh axis runs over, the one named last changes fastest.
Arguments:
- queries: bfloat16 [65536, 8192], P(('ctx', 'head')), may hold values from -13 to 13
- keys: bfloat16 [65536, 1024], P(('ctx', 'head')), may hold values from -13 to 13
- values: bfloat16 [65536, 1024], P(('ctx', 'head')), may hold values from -6 to 6
- doc_ids: int32 [65536], replicated, may hold values from 0 to 63, never falling along the last dimension, each value on 1 to 1280 neighbouring positions
Outputs:
- attended: bfloat16 [65536, 8192], P(('ctx', 'head'))
The draws below stay inside these ranges and needn't reach their ends.
Inputs may be any that keep to these rules, and one draw needn't show every extreme that they name: `doc_ids`: document numbers never fall along the sequence; every document has 1 to 1280 tokens and one has exactly 1280; every number of 0 to 63 occurs.
All inputs are finite; a program needn't handle non-finite values.
Results may differ from the reference program's by a relative error of at most 0.0025.
Values may be sent and summed in bfloat16 or wider, within the bound.
No kernel may reach another device: no remote copies, remote signals or barrier semaphores. Data moves between devices by JAX's collectives and lax.ppermute only.
A program may use at most 64 MiB of HBM per device.

```python
import math
import jax
import jax.numpy as jnp
import numpy as np
from jax import lax

HD = 128
QH = 64
KVH = 8
BLOCK = 256
DOC_BLOCKS = 5
SEQ = 65536
DOCS = 64
MOST_DOC = 1280


def draw_queries(key, part):
    scales = jnp.exp(jax.random.uniform(jax.random.fold_in(key, 31), (SEQ, QH, 1), jnp.float32, math.log(0.3), math.log(3.2)))
    entries = jnp.clip(jax.random.normal(jax.random.fold_in(key, 32), (SEQ, QH, HD), jnp.float32), -4.0, 4.0) * scales
    return entries.reshape(SEQ, QH * HD).astype(jnp.bfloat16)


def draw_keys(key, part):
    scales = jnp.exp(jax.random.uniform(jax.random.fold_in(key, 41), (SEQ, KVH, 1), jnp.float32, math.log(0.3), math.log(3.2)))
    entries = jnp.clip(jax.random.normal(jax.random.fold_in(key, 42), (SEQ, KVH, HD), jnp.float32), -4.0, 4.0) * scales
    return entries.reshape(SEQ, KVH * HD).astype(jnp.bfloat16)


def shard_levels(stream_key, extent, shards, low, high):
    loudness = 1.0
    for position, parts in shards:
        heights = jax.random.uniform(jax.random.fold_in(jax.random.fold_in(stream_key, 6), position), (parts,), jnp.float32, low / len(shards), high / len(shards))
        loudness = loudness * jnp.repeat(jnp.exp(heights), extent[position] // parts).reshape((-1,) + (1,) * (len(extent) - 1 - position))
    return loudness


def length_profile(count, total, bound, slope):
    weights = [(1 << 20) // math.isqrt(standing ** slope) + 1 for standing in range(2, count + 1)]
    surplus, holding = total - bound - (count - 1), [1] * (count - 1)
    while surplus > 0:
        free = [i for i in range(count - 1) if holding[i] < bound]
        pool, left = sum([weights[i] for i in free]), surplus
        for i in free:
            addition = min(bound - holding[i], max(1, left * weights[i] // pool), surplus)
            holding[i] = holding[i] + addition
            surplus = surplus - addition
    return np.array([bound] + holding)


def ragged_sizes(stream_key, amount, total, most, skew):
    if amount == 2:
        one = jax.random.randint(stream_key, (), max(1, total - most), min(most, total - 1) + 1)
        return jnp.stack([one, total - one])
    tallies = jnp.asarray(length_profile(amount, total, most, skew), jnp.int32)
    couples = (amount - 1) // 2
    source_of, receiver = tallies[1:1 + 2 * couples:2], tallies[2:2 + 2 * couples:2]
    slack = jnp.minimum(source_of - 1, most - receiver)
    moved = jax.random.randint(jax.random.fold_in(stream_key, 1), (couples,), 0, 1 << 20) % (slack + 1)
    tallies = tallies.at[1:1 + 2 * couples:2].set(source_of - moved).at[2:2 + 2 * couples:2].set(receiver + moved)
    return tallies[jax.random.permutation(jax.random.fold_in(stream_key, 2), amount)]


def normal_values(own_key, shape, width, reach, split=(), held_as=jnp.bfloat16):
    factor_of = shard_levels(own_key, shape, split, -0.22, 0.18) if split else 1.0
    values = jax.random.normal(own_key, shape, jnp.float32) * width * factor_of
    return jnp.minimum(jnp.maximum(values, -reach), reach).astype(held_as)


def setup_inputs(seed: int = 0) -> dict:
    splits = jax.random.split(jax.random.key(seed), 5)
    return {
        "queries": draw_queries(jax.random.fold_in(splits[4], 71), 0),
        "keys": draw_keys(jax.random.fold_in(splits[4], 71), 0),
        "values": normal_values(splits[2], (SEQ, KVH * HD), 1.0, 6.0, ((0, 512),)),
        "doc_ids": jnp.searchsorted(jnp.cumsum(ragged_sizes(splits[3], DOCS, SEQ, MOST_DOC, 2)), jnp.arange(SEQ), side="right").astype(jnp.int32),
    }


floor_score = -1e30


def attend_tile(running, query_block, key_tile, value_tile, allowed):
    maxima, totals, accum = running
    scores = jnp.einsum("qgjd,kgd->qgjk", query_block.astype(jnp.float32), key_tile.astype(jnp.float32)) * HD ** -0.5
    scores = jnp.where(allowed[:, None, None, :], scores, floor_score)
    fresh = jnp.maximum(maxima, jnp.max(scores, axis=-1))
    factor = jnp.exp(maxima - fresh)
    weights = jnp.exp(scores - fresh[..., None])
    totals = totals * factor + jnp.sum(weights, axis=-1)
    rounded = lax.optimization_barrier(weights.astype(jnp.bfloat16)).astype(jnp.float32)
    accum = accum * factor[..., None] + jnp.einsum("qgjk,kgd->qgjd", rounded, value_tile.astype(jnp.float32))
    return fresh, totals, accum


def reference(queries, keys, values, doc_ids):
    per_group = QH // KVH
    reach_tokens = DOC_BLOCKS * BLOCK
    query_blocks = queries.reshape(SEQ // BLOCK, BLOCK, KVH, per_group, HD)
    padded_keys = jnp.concatenate([jnp.zeros((reach_tokens, KVH * HD), keys.dtype), keys]).reshape(-1, BLOCK, KVH, HD)
    padded_values = jnp.concatenate([jnp.zeros((reach_tokens, KVH * HD), values.dtype), values]).reshape(-1, BLOCK, KVH, HD)
    padded_ids = jnp.concatenate([jnp.full((reach_tokens,), -1, jnp.int32), doc_ids.astype(jnp.int32)]).reshape(-1, BLOCK)
    offsets = jnp.arange(BLOCK, dtype=jnp.int32)

    def one_block(index):
        query_block = query_blocks[index]
        query_ids = padded_ids[index + DOC_BLOCKS]
        query_pos = index * BLOCK + offsets

        def visit(running, tile):
            tile_ids = padded_ids[tile]
            key_pos = (tile - DOC_BLOCKS) * BLOCK + offsets
            allowed = (query_ids[:, None] == tile_ids[None, :]) & (key_pos[None, :] <= query_pos[:, None])
            return attend_tile(running, query_block, padded_keys[tile], padded_values[tile], allowed)

        initial = (jnp.full((BLOCK, KVH, per_group), floor_score, jnp.float32),
                   jnp.zeros((BLOCK, KVH, per_group), jnp.float32),
                   jnp.zeros((BLOCK, KVH, per_group, HD), jnp.float32))
        diagonal = index + DOC_BLOCKS
        running = visit(initial, diagonal)

        def backward(offset, running):
            tile = (diagonal - offset).astype(jnp.int32)
            live = padded_ids[tile, BLOCK - 1] == query_ids[0]
            return lax.cond(live, lambda inner: visit(inner, tile), lambda inner: inner, running)

        running = lax.fori_loop(1, DOC_BLOCKS + 1, backward, running)
        maxima, totals, accum = running
        return (accum / totals[..., None]).astype(jnp.bfloat16).reshape(BLOCK, QH * HD)

    result = lax.map(one_block, jnp.arange(SEQ // BLOCK, dtype=jnp.int32))
    return result.reshape(SEQ, QH * HD)
```

```python
import functools

import jax
import jax.numpy as jnp
from jax import lax
from jax.experimental import pallas as pl
from jax.experimental.pallas import tpu as pltpu
from jax.sharding import PartitionSpec as P

HD = 128
QH = 64
KVH = 8
BLOCK = 256
DOC_BLOCKS = 5
QBLK_DEV = 4
PREV = 2


floor_score = -1e30


def from_behind(value, axis, steps):
    count = lax.axis_size(axis)
    leading, last = (max(0, -steps), min(count, count - steps))
    return lax.ppermute(value, axis, [(source, source + steps) for source in range(leading, last)])


def key_window(paired):
    pieces = []
    for offset in range(1, PREV + 1):
        pieces.append(from_behind(paired, "ctx", offset))
    return jnp.concatenate(pieces[::-1] + [paired], axis=1)


def attend_kernel(nback_ref, q_ref, k_ref, v_ref, qid_ref, kid_ref, o_ref, m_scr, l_scr, acc_scr, *, heads):
    qb = pl.program_id(0)
    step = pl.program_id(1)
    last = pl.num_programs(1) - 1

    @pl.when(step == 0)
    def _init():
        m_scr[...] = jnp.full(m_scr.shape, floor_score, jnp.float32)
        l_scr[...] = jnp.zeros(l_scr.shape, jnp.float32)
        acc_scr[...] = jnp.zeros(acc_scr.shape, jnp.float32)

    @pl.when(step <= nback_ref[qb])
    def _compute():
        allowed = qid_ref[...] == kid_ref[...]
        rows = lax.broadcasted_iota(jnp.int32, (BLOCK, BLOCK), 0)
        cols = lax.broadcasted_iota(jnp.int32, (BLOCK, BLOCK), 1)
        allowed = allowed & ((cols <= rows) | (step > 0))
        k = k_ref[...]
        v = v_ref[...]
        for j in range(heads):
            q = q_ref[:, j * HD:(j + 1) * HD]
            s = lax.dot_general(q, k, (((1,), (1,)), ((), ())), preferred_element_type=jnp.float32)
            s = s * HD ** (-0.5)
            s = jnp.where(allowed, s, floor_score)
            m_old = m_scr[j]
            m_new = jnp.maximum(m_old, jnp.max(s, axis=-1, keepdims=True))
            factor = jnp.exp(m_old - m_new)
            p = jnp.exp(s - m_new)
            l_scr[j] = l_scr[j] * factor + jnp.sum(p, axis=-1, keepdims=True)
            acc_scr[j] = acc_scr[j] * factor + jnp.dot(
                p.astype(jnp.bfloat16), v, preferred_element_type=jnp.float32)
            m_scr[j] = m_new

    @pl.when(step == last)
    def _finish():
        for j in range(heads):
            o_ref[:, j * HD:(j + 1) * HD] = (acc_scr[j] / l_scr[j]).astype(o_ref.dtype)


def attend(nback, queries, keys, values, qids, kids):
    rows, width = queries.shape
    heads = width // HD
    n_q = rows // BLOCK
    base = keys.shape[0] // BLOCK - n_q
    n_steps = DOC_BLOCKS + 1

    def kv_map(qb, step, nback_ref):
        return (base + qb - jnp.minimum(step, nback_ref[qb]), 0)

    def kid_map(qb, step, nback_ref):
        return (0, base + qb - jnp.minimum(step, nback_ref[qb]))

    grid_spec = pltpu.PrefetchScalarGridSpec(
        num_scalar_prefetch=1,
        grid=(n_q, n_steps),
        in_specs=[
            pl.BlockSpec((BLOCK, width), lambda qb, step, nb: (qb, 0)),
            pl.BlockSpec((BLOCK, HD), kv_map),
            pl.BlockSpec((BLOCK, HD), kv_map),
            pl.BlockSpec((BLOCK, 1), lambda qb, step, nb: (qb, 0)),
            pl.BlockSpec((1, BLOCK), kid_map),
        ],
        out_specs=pl.BlockSpec((BLOCK, width), lambda qb, step, nb: (qb, 0)),
        scratch_shapes=[
            pltpu.VMEM((heads, BLOCK, 1), jnp.float32),
            pltpu.VMEM((heads, BLOCK, 1), jnp.float32),
            pltpu.VMEM((heads, BLOCK, HD), jnp.float32),
        ],
    )
    flops = 4 * rows * keys.shape[0] // 2 * HD * heads
    return pl.pallas_call(
        functools.partial(attend_kernel, heads=heads),
        out_shape=jax.ShapeDtypeStruct((rows, width), queries.dtype),
        grid_spec=grid_spec,
        compiler_params=pltpu.CompilerParams(dimension_semantics=("arbitrary", "arbitrary")),
        cost_estimate=pl.CostEstimate(
            flops=flops, transcendentals=flops // (2 * HD), bytes_accessed=4 * rows * width),
    )(nback, queries, keys, values, qids, kids)


def shards(queries, keys, values, doc_ids):
    range_rows = QBLK_DEV * BLOCK
    ctx_pos = lax.axis_index("ctx")
    local_queries, local_keys, local_values = (
        lax.all_to_all(queries, "head", split_axis=1, concat_axis=0, tiled=True),
        lax.all_to_all(keys, "head", split_axis=1, concat_axis=0, tiled=True),
        lax.all_to_all(values, "head", split_axis=1, concat_axis=0, tiled=True),
    )
    window = key_window(jnp.stack([local_keys, local_values]))
    padded_ids = jnp.concatenate([jnp.full((PREV * range_rows,), -1, jnp.int32), doc_ids])
    window_ids = lax.dynamic_slice_in_dim(padded_ids, ctx_pos * range_rows, (PREV + 1) * range_rows)
    range_ids = lax.dynamic_slice_in_dim(doc_ids, ctx_pos * range_rows, range_rows)
    tile_last = window_ids.reshape(-1, BLOCK)[:, BLOCK - 1]
    first_q = range_ids.reshape(-1, BLOCK)[:, 0]
    n_q = range_rows // BLOCK
    base = PREV * n_q
    counts = []
    for qb in range(n_q):
        back = tile_last[base + qb - DOC_BLOCKS:base + qb]
        counts.append(jnp.sum((back == first_q[qb]).astype(jnp.int32)))
    nback = jnp.stack(counts)
    local_out = attend(
        nback, local_queries, window[0], window[1],
        range_ids.reshape(range_rows, 1), window_ids.reshape(1, -1))
    return lax.all_to_all(local_out, "head", split_axis=0, concat_axis=1, tiled=True)


def solution(mesh):
    in_specs = (P(("ctx", "head"), None), P(("ctx", "head"), None), P(("ctx", "head"), None), P())
    out_specs = P(("ctx", "head"), None)
    return jax.shard_map(shards, mesh=mesh, in_specs=in_specs, out_specs=out_specs, check_vma=False)
```

```python
import functools

import jax
import jax.numpy as jnp
from jax import lax
from jax.experimental import pallas as pl
from jax.experimental.pallas import tpu as pltpu
from jax.sharding import PartitionSpec as P

HD = 128
QH = 64
KVH = 8
BLOCK = 256
DOC_BLOCKS = 5
QBLK_DEV = 4
PREV = 2


floor_score = -1e30


def from_behind(value, axis, steps):
    count = lax.axis_size(axis)
    leading, last = (max(0, -steps), min(count, count - steps))
    return lax.ppermute(value, axis, [(source, source + steps) for source in range(leading, last)])


def key_window(paired):
    pieces = []
    for offset in range(1, PREV + 1):
        pieces.append(from_behind(paired, "ctx", offset))
    return jnp.concatenate(pieces[::-1] + [paired], axis=1)


def attend_kernel(nback_ref, q_ref, k_ref, v_ref, qid_ref, kid_ref, o_ref, m_scr, l_scr, acc_scr, *, heads):
    qb = pl.program_id(0)
    step = pl.program_id(1)
    last = pl.num_programs(1) - 1

    @pl.when(step == 0)
    def _init():
        m_scr[...] = jnp.full(m_scr.shape, floor_score, jnp.float32)
        l_scr[...] = jnp.zeros(l_scr.shape, jnp.float32)
        acc_scr[...] = jnp.zeros(acc_scr.shape, jnp.float32)

    def body(masked):
        k = k_ref[...]
        v = v_ref[...]
        if masked:
            allowed = qid_ref[...] == kid_ref[...]
            rows = lax.broadcasted_iota(jnp.int32, (BLOCK, BLOCK), 0)
            cols = lax.broadcasted_iota(jnp.int32, (BLOCK, BLOCK), 1)
            allowed = allowed & ((cols <= rows) | (step > 0))
        for j in range(heads):
            q = q_ref[:, j * HD:(j + 1) * HD]
            s = lax.dot_general(q, k, (((1,), (1,)), ((), ())), preferred_element_type=jnp.float32)
            s = s * HD ** (-0.5)
            if masked:
                s = jnp.where(allowed, s, floor_score)
            m_old = m_scr[j]
            m_new = jnp.maximum(m_old, jnp.max(s, axis=-1, keepdims=True))
            factor = jnp.exp(m_old - m_new)
            p = jnp.exp(s - jnp.tile(m_new, (1, BLOCK // 128)))
            l_scr[j] = l_scr[j] * factor + jnp.sum(p, axis=-1, keepdims=True)
            acc_scr[j] = acc_scr[j] * factor + jnp.dot(
                p.astype(jnp.bfloat16), v, preferred_element_type=jnp.float32)
            m_scr[j] = m_new

    @pl.when(step <= nback_ref[qb])
    def _compute():
        body(True)

    @pl.when(step == last)
    def _finish():
        for j in range(heads):
            o_ref[:, j * HD:(j + 1) * HD] = (acc_scr[j] / l_scr[j]).astype(o_ref.dtype)


def attend(nback, queries, keys, values, qids, kids):
    rows, width = queries.shape
    heads = width // HD
    n_q = rows // BLOCK
    base = keys.shape[0] // BLOCK - n_q
    n_steps = DOC_BLOCKS + 1

    def kv_map(qb, step, nback_ref):
        return (base + qb - jnp.minimum(step, nback_ref[qb]), 0)

    def kid_map(qb, step, nback_ref):
        return (0, base + qb - jnp.minimum(step, nback_ref[qb]))

    grid_spec = pltpu.PrefetchScalarGridSpec(
        num_scalar_prefetch=1,
        grid=(n_q, n_steps),
        in_specs=[
            pl.BlockSpec((BLOCK, width), lambda qb, step, nb: (qb, 0)),
            pl.BlockSpec((BLOCK, HD), kv_map),
            pl.BlockSpec((BLOCK, HD), kv_map),
            pl.BlockSpec((BLOCK, 1), lambda qb, step, nb: (qb, 0)),
            pl.BlockSpec((1, BLOCK), kid_map),
        ],
        out_specs=pl.BlockSpec((BLOCK, width), lambda qb, step, nb: (qb, 0)),
        scratch_shapes=[
            pltpu.VMEM((heads, BLOCK, 128), jnp.float32),
            pltpu.VMEM((heads, BLOCK, 128), jnp.float32),
            pltpu.VMEM((heads, BLOCK, HD), jnp.float32),
        ],
    )
    flops = 4 * rows * keys.shape[0] // 2 * HD * heads
    return pl.pallas_call(
        functools.partial(attend_kernel, heads=heads),
        out_shape=jax.ShapeDtypeStruct((rows, width), queries.dtype),
        grid_spec=grid_spec,
        compiler_params=pltpu.CompilerParams(dimension_semantics=("arbitrary", "arbitrary")),
        cost_estimate=pl.CostEstimate(
            flops=flops, transcendentals=flops // (2 * HD), bytes_accessed=4 * rows * width),
    )(nback, queries, keys, values, qids, kids)


def shards(queries, keys, values, doc_ids):
    range_rows = QBLK_DEV * BLOCK
    rows = queries.shape[0]
    heads_axis = lax.axis_size("head")
    ctx_pos = lax.axis_index("ctx")
    paired = jnp.concatenate(
        [keys.reshape(rows, heads_axis, -1), values.reshape(rows, heads_axis, -1)], axis=2)
    local_pair = lax.all_to_all(paired, "head", split_axis=1, concat_axis=0, tiled=True)
    local_queries = lax.all_to_all(queries, "head", split_axis=1, concat_axis=0, tiled=True)
    local_pair = local_pair.reshape(range_rows, 2 * HD)
    prev1 = from_behind(local_pair, "ctx", 1)
    prev2 = from_behind(local_pair[range_rows - BLOCK:], "ctx", 2)
    window = jnp.concatenate([prev2, prev1, local_pair], axis=0)
    reach = BLOCK + range_rows
    padded_ids = jnp.concatenate([jnp.full((reach,), -1, jnp.int32), doc_ids])
    window_ids = lax.dynamic_slice_in_dim(padded_ids, ctx_pos * range_rows, reach + range_rows)
    range_ids = lax.dynamic_slice_in_dim(doc_ids, ctx_pos * range_rows, range_rows)
    tile_last = window_ids.reshape(-1, BLOCK)[:, BLOCK - 1]
    first_q = range_ids.reshape(-1, BLOCK)[:, 0]
    n_q = range_rows // BLOCK
    base = reach // BLOCK
    counts = []
    for qb in range(n_q):
        lo = max(0, base + qb - DOC_BLOCKS)
        back = tile_last[lo:base + qb]
        counts.append(jnp.sum((back == first_q[qb]).astype(jnp.int32)))
    nback = jnp.stack(counts)
    local_out = attend(
        nback, local_queries, window[:, :HD], window[:, HD:],
        range_ids.reshape(range_rows, 1), window_ids.reshape(1, -1))
    return lax.all_to_all(local_out, "head", split_axis=0, concat_axis=1, tiled=True)


def solution(mesh):
    in_specs = (P(("ctx", "head"), None), P(("ctx", "head"), None), P(("ctx", "head"), None), P())
    out_specs = P(("ctx", "head"), None)
    return jax.shard_map(shards, mesh=mesh, in_specs=in_specs, out_specs=out_specs, check_vma=False)
```

```python
import functools

import jax
import jax.numpy as jnp
from jax import lax
from jax.experimental import pallas as pl
from jax.experimental.pallas import tpu as pltpu
from jax.sharding import PartitionSpec as P

HD = 128
QH = 64
KVH = 8
BLOCK = 256
DOC_BLOCKS = 5
QBLK_DEV = 4
PREV = 2


floor_score = -1e30


def from_behind(value, axis, steps):
    count = lax.axis_size(axis)
    leading, last = (max(0, -steps), min(count, count - steps))
    return lax.ppermute(value, axis, [(source, source + steps) for source in range(leading, last)])


def key_window(paired):
    pieces = []
    for offset in range(1, PREV + 1):
        pieces.append(from_behind(paired, "ctx", offset))
    return jnp.concatenate(pieces[::-1] + [paired], axis=1)


def attend_kernel(nback_ref, q_ref, k_ref, v_ref, qid_ref, kid_ref, o_ref, m_scr, l_scr, acc_scr, *, heads):
    qb = pl.program_id(0)
    step = pl.program_id(1)
    last = pl.num_programs(1) - 1

    @pl.when(step == 0)
    def _init():
        m_scr[...] = jnp.full(m_scr.shape, floor_score, jnp.float32)
        l_scr[...] = jnp.zeros(l_scr.shape, jnp.float32)
        acc_scr[...] = jnp.zeros(acc_scr.shape, jnp.float32)

    def body(masked):
        k = k_ref[...]
        v = v_ref[...]
        if masked:
            allowed = qid_ref[...] == kid_ref[...]
            rows = lax.broadcasted_iota(jnp.int32, (BLOCK, BLOCK), 0)
            cols = lax.broadcasted_iota(jnp.int32, (BLOCK, BLOCK), 1)
            allowed = allowed & ((cols <= rows) | (step > 0))
        for j in range(heads):
            q = q_ref[:, j * HD:(j + 1) * HD]
            s = lax.dot_general(q, k, (((1,), (1,)), ((), ())), preferred_element_type=jnp.float32)
            s = s * HD ** (-0.5)
            if masked:
                s = jnp.where(allowed, s, floor_score)
            m_old = m_scr[j]
            m_new = jnp.maximum(m_old, jnp.max(s, axis=-1, keepdims=True))
            factor = jnp.exp(m_old - m_new)
            p = jnp.exp(s - jnp.tile(m_new, (1, BLOCK // 128)))
            l_scr[j] = l_scr[j] * factor + jnp.sum(p, axis=-1, keepdims=True)
            acc_scr[j] = acc_scr[j] * factor + jnp.dot(
                p.astype(jnp.bfloat16), v, preferred_element_type=jnp.float32)
            m_scr[j] = m_new

    @pl.when(step <= nback_ref[qb])
    def _compute():
        body(True)

    @pl.when(step == last)
    def _finish():
        for j in range(heads):
            o_ref[:, j * HD:(j + 1) * HD] = (acc_scr[j] / l_scr[j]).astype(o_ref.dtype)


def attend(nback, queries, keys, values, qids, kids):
    rows, width = queries.shape
    heads = width // HD
    n_q = rows // BLOCK
    base = keys.shape[0] // BLOCK - n_q
    n_steps = DOC_BLOCKS + 1

    def kv_map(qb, step, nback_ref):
        return (base + qb - jnp.minimum(step, nback_ref[qb]), 0)

    def kid_map(qb, step, nback_ref):
        return (0, base + qb - jnp.minimum(step, nback_ref[qb]))

    grid_spec = pltpu.PrefetchScalarGridSpec(
        num_scalar_prefetch=1,
        grid=(n_q, n_steps),
        in_specs=[
            pl.BlockSpec((BLOCK, width), lambda qb, step, nb: (qb, 0)),
            pl.BlockSpec((BLOCK, HD), kv_map),
            pl.BlockSpec((BLOCK, HD), kv_map),
            pl.BlockSpec((BLOCK, 1), lambda qb, step, nb: (qb, 0)),
            pl.BlockSpec((1, BLOCK), kid_map),
        ],
        out_specs=pl.BlockSpec((BLOCK, width), lambda qb, step, nb: (qb, 0)),
        scratch_shapes=[
            pltpu.VMEM((heads, BLOCK, 128), jnp.float32),
            pltpu.VMEM((heads, BLOCK, 128), jnp.float32),
            pltpu.VMEM((heads, BLOCK, HD), jnp.float32),
        ],
    )
    flops = 4 * rows * keys.shape[0] // 2 * HD * heads
    return pl.pallas_call(
        functools.partial(attend_kernel, heads=heads),
        out_shape=jax.ShapeDtypeStruct((rows, width), queries.dtype),
        grid_spec=grid_spec,
        compiler_params=pltpu.CompilerParams(dimension_semantics=("arbitrary", "arbitrary")),
        cost_estimate=pl.CostEstimate(
            flops=flops, transcendentals=flops // (2 * HD), bytes_accessed=4 * rows * width),
    )(nback, queries, keys, values, qids, kids)


SPLIT = 2


def exchange(pieces_for, axis):
    count = lax.axis_size(axis)
    got = [pieces_for(0)]
    for d in range(1, count):
        perm = [(src, (src + d) % count) for src in range(count)]
        got.append(lax.ppermute(pieces_for(d), axis, perm))
    return jnp.stack(got)


def by_source(stacked, me, count):
    order = (me - jnp.arange(count, dtype=jnp.int32)) % count
    return jnp.take(stacked, order, axis=0)


def shards(queries, keys, values, doc_ids):
    range_rows = QBLK_DEV * BLOCK
    rows = queries.shape[0]
    n_head = lax.axis_size("head")
    me = lax.axis_index("head")
    ctx_pos = lax.axis_index("ctx")
    per_group = QH // KVH
    part = per_group // SPLIT
    grouped_q = queries.reshape(rows, n_head, SPLIT, part * HD)
    paired = jnp.concatenate(
        [keys.reshape(rows, n_head, HD), values.reshape(rows, n_head, HD)], axis=2)

    def group_piece(array, d):
        return lax.dynamic_index_in_dim(array, (me + d) % n_head, axis=1, keepdims=False)

    local_pair = by_source(exchange(lambda d: group_piece(paired, d), "head"), me, n_head)
    local_pair = local_pair.reshape(range_rows, 2 * HD)
    local_qs = []
    for s in range(SPLIT):
        got = exchange(lambda d: group_piece(grouped_q[:, :, s], d), "head")
        local_qs.append(by_source(got, me, n_head).reshape(range_rows, part * HD))
    prev1 = from_behind(local_pair, "ctx", 1)
    prev2 = from_behind(local_pair[range_rows - BLOCK:], "ctx", 2)
    window = jnp.concatenate([prev2, prev1, local_pair], axis=0)
    reach = BLOCK + range_rows
    padded_ids = jnp.concatenate([jnp.full((reach,), -1, jnp.int32), doc_ids])
    window_ids = lax.dynamic_slice_in_dim(padded_ids, ctx_pos * range_rows, reach + range_rows)
    range_ids = lax.dynamic_slice_in_dim(doc_ids, ctx_pos * range_rows, range_rows)
    tile_last = window_ids.reshape(-1, BLOCK)[:, BLOCK - 1]
    first_q = range_ids.reshape(-1, BLOCK)[:, 0]
    n_q = range_rows // BLOCK
    base = reach // BLOCK
    counts = []
    for qb in range(n_q):
        lo = max(0, base + qb - DOC_BLOCKS)
        back = tile_last[lo:base + qb]
        counts.append(jnp.sum((back == first_q[qb]).astype(jnp.int32)))
    nback = jnp.stack(counts)
    qids = range_ids.reshape(range_rows, 1)
    kids = window_ids.reshape(1, -1)
    outs = []
    for s in range(SPLIT):
        local_out = attend(nback, local_qs[s], window[:, :HD], window[:, HD:], qids, kids)
        chunks = local_out.reshape(n_head, rows, part * HD)
        got = exchange(lambda d: lax.dynamic_index_in_dim(chunks, (me + d) % n_head, 0, False), "head")
        outs.append(by_source(got, me, n_head))
    full = jnp.stack(outs, axis=2)
    return jnp.transpose(full, (1, 0, 2, 3)).reshape(rows, QH * HD)


def solution(mesh):
    in_specs = (P(("ctx", "head"), None), P(("ctx", "head"), None), P(("ctx", "head"), None), P())
    out_specs = P(("ctx", "head"), None)
    return jax.shard_map(shards, mesh=mesh, in_specs=in_specs, out_specs=out_specs, check_vma=False)
```

```python
import functools

import jax
import jax.numpy as jnp
from jax import lax
from jax.experimental import pallas as pl
from jax.experimental.pallas import tpu as pltpu
from jax.sharding import PartitionSpec as P

HD = 128
QH = 64
KVH = 8
BLOCK = 256
DOC_BLOCKS = 5
QBLK_DEV = 4
PREV = 2


floor_score = -1e30


def from_behind(value, axis, steps):
    count = lax.axis_size(axis)
    leading, last = (max(0, -steps), min(count, count - steps))
    return lax.ppermute(value, axis, [(source, source + steps) for source in range(leading, last)])


def key_window(paired):
    pieces = []
    for offset in range(1, PREV + 1):
        pieces.append(from_behind(paired, "ctx", offset))
    return jnp.concatenate(pieces[::-1] + [paired], axis=1)


def attend_kernel(nback_ref, q_ref, k_ref, v_ref, qid_ref, kid_ref, o_ref, m_scr, l_scr, acc_scr, *, heads):
    qb = pl.program_id(0)
    step = pl.program_id(1)
    last = pl.num_programs(1) - 1

    @pl.when(step == 0)
    def _init():
        m_scr[...] = jnp.full(m_scr.shape, floor_score, jnp.float32)
        l_scr[...] = jnp.zeros(l_scr.shape, jnp.float32)
        acc_scr[...] = jnp.zeros(acc_scr.shape, jnp.float32)

    def body(masked):
        k = k_ref[...]
        v = v_ref[...]
        if masked:
            allowed = qid_ref[...] == kid_ref[...]
            rows = lax.broadcasted_iota(jnp.int32, (BLOCK, BLOCK), 0)
            cols = lax.broadcasted_iota(jnp.int32, (BLOCK, BLOCK), 1)
            allowed = allowed & ((cols <= rows) | (step > 0))
        for j in range(heads):
            q = q_ref[:, j * HD:(j + 1) * HD]
            s = lax.dot_general(q, k, (((1,), (1,)), ((), ())), preferred_element_type=jnp.float32)
            s = s * HD ** (-0.5)
            if masked:
                s = jnp.where(allowed, s, floor_score)
            m_old = m_scr[j]
            m_new = jnp.maximum(m_old, jnp.max(s, axis=-1, keepdims=True))
            factor = jnp.exp(m_old - m_new)
            p = jnp.exp(s - jnp.tile(m_new, (1, BLOCK // 128)))
            l_scr[j] = l_scr[j] * factor + jnp.sum(p, axis=-1, keepdims=True)
            acc_scr[j] = acc_scr[j] * factor + jnp.dot(
                p.astype(jnp.bfloat16), v, preferred_element_type=jnp.float32)
            m_scr[j] = m_new

    @pl.when(step <= nback_ref[qb])
    def _compute():
        body(True)

    @pl.when(step == last)
    def _finish():
        for j in range(heads):
            o_ref[:, j * HD:(j + 1) * HD] = (acc_scr[j] / l_scr[j]).astype(o_ref.dtype)


def attend(nback, queries, keys, values, qids, kids):
    rows, width = queries.shape
    heads = width // HD
    n_q = rows // BLOCK
    base = keys.shape[0] // BLOCK - n_q
    n_steps = DOC_BLOCKS + 1

    def kv_map(qb, step, nback_ref):
        return (base + qb - jnp.minimum(step, nback_ref[qb]), 0)

    def kid_map(qb, step, nback_ref):
        return (0, base + qb - jnp.minimum(step, nback_ref[qb]))

    grid_spec = pltpu.PrefetchScalarGridSpec(
        num_scalar_prefetch=1,
        grid=(n_q, n_steps),
        in_specs=[
            pl.BlockSpec((BLOCK, width), lambda qb, step, nb: (qb, 0)),
            pl.BlockSpec((BLOCK, HD), kv_map),
            pl.BlockSpec((BLOCK, HD), kv_map),
            pl.BlockSpec((BLOCK, 1), lambda qb, step, nb: (qb, 0)),
            pl.BlockSpec((1, BLOCK), kid_map),
        ],
        out_specs=pl.BlockSpec((BLOCK, width), lambda qb, step, nb: (qb, 0)),
        scratch_shapes=[
            pltpu.VMEM((heads, BLOCK, 128), jnp.float32),
            pltpu.VMEM((heads, BLOCK, 128), jnp.float32),
            pltpu.VMEM((heads, BLOCK, HD), jnp.float32),
        ],
    )
    flops = 40 * rows * keys.shape[0] // 2 * HD * heads
    return pl.pallas_call(
        functools.partial(attend_kernel, heads=heads),
        out_shape=jax.ShapeDtypeStruct((rows, width), queries.dtype),
        grid_spec=grid_spec,
        compiler_params=pltpu.CompilerParams(dimension_semantics=("arbitrary", "arbitrary")),
        cost_estimate=pl.CostEstimate(
            flops=flops, transcendentals=flops // (2 * HD), bytes_accessed=4 * rows * width),
    )(nback, queries, keys, values, qids, kids)


SPLIT = 2


def shards(queries, keys, values, doc_ids):
    range_rows = QBLK_DEV * BLOCK
    rows = queries.shape[0]
    n_head = lax.axis_size("head")
    ctx_pos = lax.axis_index("ctx")
    part = (QH // KVH) // SPLIT
    grouped_q = queries.reshape(rows, n_head, SPLIT, part * HD)
    first = jnp.concatenate(
        [keys.reshape(rows, n_head, HD), values.reshape(rows, n_head, HD), grouped_q[:, :, 0]], axis=2)
    first = lax.all_to_all(first, "head", split_axis=1, concat_axis=0, tiled=True)
    first = first.reshape(range_rows, 2 * HD + part * HD)
    local_pair = first[:, :2 * HD]
    local_qs = [first[:, 2 * HD:]]
    for s in range(1, SPLIT):
        got = lax.all_to_all(grouped_q[:, :, s], "head", split_axis=1, concat_axis=0, tiled=True)
        local_qs.append(got.reshape(range_rows, part * HD))
    prev1 = from_behind(local_pair, "ctx", 1)
    prev2 = from_behind(local_pair[range_rows - BLOCK:], "ctx", 2)
    window = jnp.concatenate([prev2, prev1, local_pair], axis=0)
    reach = BLOCK + range_rows
    padded_ids = jnp.concatenate([jnp.full((reach,), -1, jnp.int32), doc_ids])
    window_ids = lax.dynamic_slice_in_dim(padded_ids, ctx_pos * range_rows, reach + range_rows)
    range_ids = lax.dynamic_slice_in_dim(doc_ids, ctx_pos * range_rows, range_rows)
    tile_last = window_ids.reshape(-1, BLOCK)[:, BLOCK - 1]
    first_q = range_ids.reshape(-1, BLOCK)[:, 0]
    n_q = range_rows // BLOCK
    base = reach // BLOCK
    counts = []
    for qb in range(n_q):
        lo = max(0, base + qb - DOC_BLOCKS)
        back = tile_last[lo:base + qb]
        counts.append(jnp.sum((back == first_q[qb]).astype(jnp.int32)))
    nback = jnp.stack(counts)
    qids = range_ids.reshape(range_rows, 1)
    kids = window_ids.reshape(1, -1)
    window_keys, window_values = window[:, :HD], window[:, HD:]
    outs = []
    local_out = None
    for s in range(SPLIT):
        q_s = local_qs[s]
        if local_out is not None:
            outs.append(lax.all_to_all(
                local_out.reshape(range_rows, 1, part * HD), "head", split_axis=0, concat_axis=1, tiled=True))
            q_s, _ = lax.optimization_barrier((q_s, local_out))
        local_out = attend(nback, q_s, window_keys, window_values, qids, kids)
    outs.append(lax.all_to_all(
        local_out.reshape(range_rows, 1, part * HD), "head", split_axis=0, concat_axis=1, tiled=True))
    full = jnp.stack(outs, axis=2)
    return full.reshape(rows, QH * HD)


def solution(mesh):
    in_specs = (P(("ctx", "head"), None), P(("ctx", "head"), None), P(("ctx", "head"), None), P())
    out_specs = P(("ctx", "head"), None)
    return jax.shard_map(shards, mesh=mesh, in_specs=in_specs, out_specs=out_specs, check_vma=False)
```

```python
import functools

import jax
import jax.numpy as jnp
from jax import lax
from jax.experimental import pallas as pl
from jax.experimental.pallas import tpu as pltpu
from jax.sharding import PartitionSpec as P

HD = 128
QH = 64
KVH = 8
BLOCK = 256
DOC_BLOCKS = 5
QBLK_DEV = 4
PREV = 2
MXU_SUM = True


floor_score = -1e30


def from_behind(value, axis, steps):
    count = lax.axis_size(axis)
    leading, last = (max(0, -steps), min(count, count - steps))
    return lax.ppermute(value, axis, [(source, source + steps) for source in range(leading, last)])


def key_window(paired):
    pieces = []
    for offset in range(1, PREV + 1):
        pieces.append(from_behind(paired, "ctx", offset))
    return jnp.concatenate(pieces[::-1] + [paired], axis=1)


def attend_kernel(nback_ref, full_ref, q_ref, k_ref, v_ref, qid_ref, kid_ref, o_ref, m_scr, l_scr, acc_scr, *, heads, n_steps, mxu_sum):
    qb = pl.program_id(0)
    step = pl.program_id(1)
    last = pl.num_programs(1) - 1

    @pl.when(step == 0)
    def _init():
        m_scr[...] = jnp.full(m_scr.shape, floor_score, jnp.float32)
        if not mxu_sum:
            l_scr[...] = jnp.zeros(l_scr.shape, jnp.float32)
        acc_scr[...] = jnp.zeros(acc_scr.shape, jnp.float32)

    def body(masked):
        k = k_ref[...]
        v = v_ref[...]
        if mxu_sum:
            v = jnp.concatenate([v, jnp.ones_like(v)], axis=1)
        if masked:
            allowed = qid_ref[...] == kid_ref[...]
            rows = lax.broadcasted_iota(jnp.int32, (BLOCK, BLOCK), 0)
            cols = lax.broadcasted_iota(jnp.int32, (BLOCK, BLOCK), 1)
            allowed = allowed & ((cols <= rows) | (step > 0))
        for j in range(heads):
            q = q_ref[:, j * HD:(j + 1) * HD]
            s = lax.dot_general(q, k, (((1,), (1,)), ((), ())), preferred_element_type=jnp.float32)
            s = s * HD ** (-0.5)
            if masked:
                s = jnp.where(allowed, s, floor_score)
            m_old = m_scr[j]
            m_new = jnp.maximum(m_old, jnp.max(s, axis=-1, keepdims=True))
            factor = jnp.exp(m_old - m_new)
            p = jnp.exp(s - jnp.tile(m_new, (1, BLOCK // 128)))
            pv = jnp.dot(p.astype(jnp.bfloat16), v, preferred_element_type=jnp.float32)
            if mxu_sum:
                acc_scr[j] = acc_scr[j] * jnp.tile(factor, (1, 2)) + pv
            else:
                l_scr[j] = l_scr[j] * factor + jnp.sum(p, axis=-1, keepdims=True)
                acc_scr[j] = acc_scr[j] * factor + pv
            m_scr[j] = m_new

    live = step <= nback_ref[qb]
    full = full_ref[qb * n_steps + step] > 0

    @pl.when(live & full)
    def _plain():
        body(False)

    @pl.when(live & jnp.logical_not(full))
    def _masked():
        body(True)

    @pl.when(step == last)
    def _finish():
        for j in range(heads):
            if mxu_sum:
                total = acc_scr[j, :, HD:]
                o_ref[:, j * HD:(j + 1) * HD] = (acc_scr[j, :, :HD] / total).astype(o_ref.dtype)
            else:
                o_ref[:, j * HD:(j + 1) * HD] = (acc_scr[j] / l_scr[j]).astype(o_ref.dtype)


def attend(nback, full, queries, keys, values, qids, kids, mxu_sum=MXU_SUM):
    rows, width = queries.shape
    heads = width // HD
    n_q = rows // BLOCK
    base = keys.shape[0] // BLOCK - n_q
    n_steps = DOC_BLOCKS + 1

    def kv_map(qb, step, nback_ref, full_ref):
        return (base + qb - jnp.minimum(step, nback_ref[qb]), 0)

    def kid_map(qb, step, nback_ref, full_ref):
        return (0, base + qb - jnp.minimum(step, nback_ref[qb]))

    grid_spec = pltpu.PrefetchScalarGridSpec(
        num_scalar_prefetch=2,
        grid=(n_q, n_steps),
        in_specs=[
            pl.BlockSpec((BLOCK, width), lambda qb, step, nb, fl: (qb, 0)),
            pl.BlockSpec((BLOCK, HD), kv_map),
            pl.BlockSpec((BLOCK, HD), kv_map),
            pl.BlockSpec((BLOCK, 1), lambda qb, step, nb, fl: (qb, 0)),
            pl.BlockSpec((1, BLOCK), kid_map),
        ],
        out_specs=pl.BlockSpec((BLOCK, width), lambda qb, step, nb, fl: (qb, 0)),
        scratch_shapes=[
            pltpu.VMEM((heads, BLOCK, 128), jnp.float32),
            pltpu.VMEM((heads, BLOCK, 128), jnp.float32),
            pltpu.VMEM((heads, BLOCK, 2 * HD if mxu_sum else HD), jnp.float32),
        ],
    )
    flops = 40 * rows * keys.shape[0] // 2 * HD * heads
    return pl.pallas_call(
        functools.partial(attend_kernel, heads=heads, n_steps=n_steps, mxu_sum=mxu_sum),
        out_shape=jax.ShapeDtypeStruct((rows, width), queries.dtype),
        grid_spec=grid_spec,
        compiler_params=pltpu.CompilerParams(dimension_semantics=("arbitrary", "arbitrary")),
        cost_estimate=pl.CostEstimate(
            flops=flops, transcendentals=flops // (20 * HD), bytes_accessed=4 * rows * width),
    )(nback, full, queries, keys, values, qids, kids)


def shards(queries, keys, values, doc_ids):
    range_rows = QBLK_DEV * BLOCK
    rows = queries.shape[0]
    heads_axis = lax.axis_size("head")
    ctx_pos = lax.axis_index("ctx")
    paired = jnp.concatenate(
        [keys.reshape(rows, heads_axis, -1), values.reshape(rows, heads_axis, -1)], axis=2)
    local_pair = lax.all_to_all(paired, "head", split_axis=1, concat_axis=0, tiled=True)
    local_queries = lax.all_to_all(queries, "head", split_axis=1, concat_axis=0, tiled=True)
    local_pair = local_pair.reshape(range_rows, 2 * HD)
    prev1 = from_behind(local_pair, "ctx", 1)
    prev2 = from_behind(local_pair[range_rows - BLOCK:], "ctx", 2)
    window = jnp.concatenate([prev2, prev1, local_pair], axis=0)
    reach = BLOCK + range_rows
    padded_ids = jnp.concatenate([jnp.full((reach,), -1, jnp.int32), doc_ids])
    window_ids = lax.dynamic_slice_in_dim(padded_ids, ctx_pos * range_rows, reach + range_rows)
    range_ids = lax.dynamic_slice_in_dim(doc_ids, ctx_pos * range_rows, range_rows)
    tile_last = window_ids.reshape(-1, BLOCK)[:, BLOCK - 1]
    first_q = range_ids.reshape(-1, BLOCK)[:, 0]
    n_q = range_rows // BLOCK
    base = reach // BLOCK
    counts = []
    for qb in range(n_q):
        lo = max(0, base + qb - DOC_BLOCKS)
        back = tile_last[lo:base + qb]
        counts.append(jnp.sum((back == first_q[qb]).astype(jnp.int32)))
    nback = jnp.stack(counts)
    tile_first = window_ids.reshape(-1, BLOCK)[:, 0]
    last_q = range_ids.reshape(-1, BLOCK)[:, BLOCK - 1]
    flags = []
    for qb in range(n_q):
        for step in range(DOC_BLOCKS + 1):
            tile = base + qb - step
            if step == 0 or tile < 0:
                flags.append(jnp.zeros((), jnp.int32))
            else:
                flags.append((tile_first[tile] == last_q[qb]).astype(jnp.int32))
    full = jnp.stack(flags)
    local_out = attend(
        nback, full, local_queries, window[:, :HD], window[:, HD:],
        range_ids.reshape(range_rows, 1), window_ids.reshape(1, -1))
    return lax.all_to_all(local_out, "head", split_axis=0, concat_axis=1, tiled=True)


def solution(mesh):
    in_specs = (P(("ctx", "head"), None), P(("ctx", "head"), None), P(("ctx", "head"), None), P())
    out_specs = P(("ctx", "head"), None)
    return jax.shard_map(shards, mesh=mesh, in_specs=in_specs, out_specs=out_specs, check_vma=False)
```

```python
import functools

import numpy as np

import jax
import jax.numpy as jnp
from jax import lax
from jax.experimental import pallas as pl
from jax.experimental.pallas import tpu as pltpu
from jax.sharding import PartitionSpec as P

HD = 128
QH = 64
KVH = 8
BLOCK = 256
DOC_BLOCKS = 5
QBLK_DEV = 4
PREV = 2
MXU_SUM = True


floor_score = -1e30


def from_behind(value, axis, steps):
    count = lax.axis_size(axis)
    leading, last = (max(0, -steps), min(count, count - steps))
    return lax.ppermute(value, axis, [(source, source + steps) for source in range(leading, last)])


def key_window(paired):
    pieces = []
    for offset in range(1, PREV + 1):
        pieces.append(from_behind(paired, "ctx", offset))
    return jnp.concatenate(pieces[::-1] + [paired], axis=1)


def attend_kernel(nback_ref, full_ref, q_ref, k_ref, v_ref, qid_ref, kid_ref, o_ref, m_scr, l_scr, acc_scr, *, heads, n_steps, mxu_sum):
    qb = pl.program_id(0)
    step = pl.program_id(1)
    last = pl.num_programs(1) - 1

    @pl.when(step == 0)
    def _init():
        m_scr[...] = jnp.full(m_scr.shape, floor_score, jnp.float32)
        if not mxu_sum:
            l_scr[...] = jnp.zeros(l_scr.shape, jnp.float32)
        acc_scr[...] = jnp.zeros(acc_scr.shape, jnp.float32)

    def body(masked):
        k = k_ref[...]
        v = v_ref[...]
        if mxu_sum:
            v = jnp.concatenate([v, jnp.ones_like(v)], axis=1)
        if masked:
            allowed = qid_ref[...] == kid_ref[...]
            rows = lax.broadcasted_iota(jnp.int32, (BLOCK, BLOCK), 0)
            cols = lax.broadcasted_iota(jnp.int32, (BLOCK, BLOCK), 1)
            allowed = allowed & ((cols <= rows) | (step > 0))
        for j in range(heads):
            q = q_ref[:, j * HD:(j + 1) * HD]
            s = lax.dot_general(q, k, (((1,), (1,)), ((), ())), preferred_element_type=jnp.float32)
            s = s * HD ** (-0.5)
            if masked:
                s = jnp.where(allowed, s, floor_score)
            m_old = m_scr[j]
            m_new = jnp.maximum(m_old, jnp.max(s, axis=-1, keepdims=True))
            factor = jnp.exp(m_old - m_new)
            p = jnp.exp(s - jnp.tile(m_new, (1, BLOCK // 128)))
            pv = jnp.dot(p.astype(jnp.bfloat16), v, preferred_element_type=jnp.float32)
            if mxu_sum:
                acc_scr[j] = acc_scr[j] * jnp.tile(factor, (1, 2)) + pv
            else:
                l_scr[j] = l_scr[j] * factor + jnp.sum(p, axis=-1, keepdims=True)
                acc_scr[j] = acc_scr[j] * factor + pv
            m_scr[j] = m_new

    live = step <= nback_ref[qb]
    full = full_ref[qb * n_steps + step] > 0

    @pl.when(live & full)
    def _plain():
        body(False)

    @pl.when(live & jnp.logical_not(full))
    def _masked():
        body(True)

    @pl.when(step == last)
    def _finish():
        for j in range(heads):
            if mxu_sum:
                total = acc_scr[j, :, HD:]
                o_ref[:, j * HD:(j + 1) * HD] = (acc_scr[j, :, :HD] / total).astype(o_ref.dtype)
            else:
                o_ref[:, j * HD:(j + 1) * HD] = (acc_scr[j] / l_scr[j]).astype(o_ref.dtype)


def attend(nback, full, queries, keys, values, qids, kids, mxu_sum=MXU_SUM):
    rows, width = queries.shape
    heads = width // HD
    n_q = rows // BLOCK
    base = keys.shape[0] // BLOCK - n_q
    n_steps = DOC_BLOCKS + 1

    def kv_map(qb, step, nback_ref, full_ref):
        return (base + qb - jnp.minimum(step, nback_ref[qb]), 0)

    def kid_map(qb, step, nback_ref, full_ref):
        return (0, base + qb - jnp.minimum(step, nback_ref[qb]))

    grid_spec = pltpu.PrefetchScalarGridSpec(
        num_scalar_prefetch=2,
        grid=(n_q, n_steps),
        in_specs=[
            pl.BlockSpec((BLOCK, width), lambda qb, step, nb, fl: (qb, 0)),
            pl.BlockSpec((BLOCK, HD), kv_map),
            pl.BlockSpec((BLOCK, HD), kv_map),
            pl.BlockSpec((BLOCK, 1), lambda qb, step, nb, fl: (qb, 0)),
            pl.BlockSpec((1, BLOCK), kid_map),
        ],
        out_specs=pl.BlockSpec((BLOCK, width), lambda qb, step, nb, fl: (qb, 0)),
        scratch_shapes=[
            pltpu.VMEM((heads, BLOCK, 128), jnp.float32),
            pltpu.VMEM((heads, BLOCK, 128), jnp.float32),
            pltpu.VMEM((heads, BLOCK, 2 * HD if mxu_sum else HD), jnp.float32),
        ],
    )
    flops = 40 * rows * keys.shape[0] // 2 * HD * heads
    return pl.pallas_call(
        functools.partial(attend_kernel, heads=heads, n_steps=n_steps, mxu_sum=mxu_sum),
        out_shape=jax.ShapeDtypeStruct((rows, width), queries.dtype),
        grid_spec=grid_spec,
        compiler_params=pltpu.CompilerParams(dimension_semantics=("arbitrary", "arbitrary")),
        cost_estimate=pl.CostEstimate(
            flops=flops, transcendentals=flops // (20 * HD), bytes_accessed=4 * rows * width),
    )(nback, full, queries, keys, values, qids, kids)


def shards(queries, keys, values, doc_ids):
    range_rows = QBLK_DEV * BLOCK
    rows = queries.shape[0]
    heads_axis = lax.axis_size("head")
    ctx_pos = lax.axis_index("ctx")
    paired = jnp.concatenate(
        [keys.reshape(rows, heads_axis, -1), values.reshape(rows, heads_axis, -1)], axis=2)
    local_pair = lax.all_to_all(paired, "head", split_axis=1, concat_axis=0, tiled=True)
    local_queries = lax.all_to_all(queries, "head", split_axis=1, concat_axis=0, tiled=True)
    local_pair = local_pair.reshape(range_rows, 2 * HD)
    prev1 = from_behind(local_pair, "ctx", 1)
    prev2 = from_behind(local_pair[range_rows - BLOCK:], "ctx", 2)
    window = jnp.concatenate([prev2, prev1, local_pair], axis=0)
    reach = BLOCK + range_rows
    n_q = range_rows // BLOCK
    n_steps = DOC_BLOCKS + 1
    base = reach // BLOCK
    window_start = ctx_pos * range_rows - reach
    positions = window_start + jnp.arange(reach + range_rows, dtype=jnp.int32)
    window_ids = lax.dynamic_slice_in_dim(doc_ids, jnp.maximum(window_start, 0), reach + range_rows)
    shift = jnp.minimum(window_start, 0)
    window_ids = jnp.where(positions < 0, -1, jnp.roll(window_ids, -shift))
    range_ids = window_ids[reach:]
    tile_first = window_ids.reshape(-1, BLOCK)[:, 0]
    tile_last = window_ids.reshape(-1, BLOCK)[:, BLOCK - 1]
    first_q = range_ids.reshape(-1, BLOCK)[:, 0]
    last_q = range_ids.reshape(-1, BLOCK)[:, BLOCK - 1]
    steps = np.arange(n_steps)
    tiles = base + np.arange(n_q)[:, None] - steps[None, :]
    live = (tile_last[tiles] == first_q[:, None]) & (steps[None, :] > 0)
    nback = jnp.sum(live.astype(jnp.int32), axis=1)
    full = ((tile_first[tiles] == last_q[:, None]) & (steps[None, :] > 0)).astype(jnp.int32).reshape(-1)
    local_out = attend(
        nback, full, local_queries, window[:, :HD], window[:, HD:],
        range_ids.reshape(range_rows, 1), window_ids.reshape(1, -1))
    return lax.all_to_all(local_out, "head", split_axis=0, concat_axis=1, tiled=True)


def solution(mesh):
    in_specs = (P(("ctx", "head"), None), P(("ctx", "head"), None), P(("ctx", "head"), None), P())
    out_specs = P(("ctx", "head"), None)
    return jax.shard_map(shards, mesh=mesh, in_specs=in_specs, out_specs=out_specs, check_vma=False)
```

```python
import functools

import numpy as np

import jax
import jax.numpy as jnp
from jax import lax
from jax.experimental import pallas as pl
from jax.experimental.pallas import tpu as pltpu
from jax.sharding import PartitionSpec as P

HD = 128
QH = 64
KVH = 8
BLOCK = 256
DOC_BLOCKS = 5
QBLK_DEV = 4
PREV = 2
MXU_SUM = True
SPLIT = 2


floor_score = -1e30


def from_behind(value, axis, steps):
    count = lax.axis_size(axis)
    leading, last = (max(0, -steps), min(count, count - steps))
    return lax.ppermute(value, axis, [(source, source + steps) for source in range(leading, last)])


def key_window(paired):
    pieces = []
    for offset in range(1, PREV + 1):
        pieces.append(from_behind(paired, "ctx", offset))
    return jnp.concatenate(pieces[::-1] + [paired], axis=1)


def attend_kernel(nback_ref, full_ref, q_ref, k_ref, v_ref, qid_ref, kid_ref, o_ref, m_scr, l_scr, acc_scr, *, heads, n_steps, mxu_sum):
    qb = pl.program_id(0)
    step = pl.program_id(1)
    last = pl.num_programs(1) - 1

    @pl.when(step == 0)
    def _init():
        m_scr[...] = jnp.full(m_scr.shape, floor_score, jnp.float32)
        if not mxu_sum:
            l_scr[...] = jnp.zeros(l_scr.shape, jnp.float32)
        acc_scr[...] = jnp.zeros(acc_scr.shape, jnp.float32)

    def body(masked):
        k = k_ref[...]
        v = v_ref[...]
        if mxu_sum:
            v = jnp.concatenate([v, jnp.ones_like(v)], axis=1)
        if masked:
            allowed = qid_ref[...] == kid_ref[...]
            rows = lax.broadcasted_iota(jnp.int32, (BLOCK, BLOCK), 0)
            cols = lax.broadcasted_iota(jnp.int32, (BLOCK, BLOCK), 1)
            allowed = allowed & ((cols <= rows) | (step > 0))
        for j in range(heads):
            q = q_ref[:, j * HD:(j + 1) * HD]
            s = lax.dot_general(q, k, (((1,), (1,)), ((), ())), preferred_element_type=jnp.float32)
            s = s * HD ** (-0.5)
            if masked:
                s = jnp.where(allowed, s, floor_score)
            m_old = m_scr[j]
            m_new = jnp.maximum(m_old, jnp.max(s, axis=-1, keepdims=True))
            factor = jnp.exp(m_old - m_new)
            p = jnp.exp(s - jnp.tile(m_new, (1, BLOCK // 128)))
            pv = jnp.dot(p.astype(jnp.bfloat16), v, preferred_element_type=jnp.float32)
            if mxu_sum:
                acc_scr[j] = acc_scr[j] * jnp.tile(factor, (1, 2)) + pv
            else:
                l_scr[j] = l_scr[j] * factor + jnp.sum(p, axis=-1, keepdims=True)
                acc_scr[j] = acc_scr[j] * factor + pv
            m_scr[j] = m_new

    live = step <= nback_ref[qb]
    full = full_ref[qb * n_steps + step] > 0

    @pl.when(live & full)
    def _plain():
        body(False)

    @pl.when(live & jnp.logical_not(full))
    def _masked():
        body(True)

    @pl.when(step == last)
    def _finish():
        for j in range(heads):
            if mxu_sum:
                total = acc_scr[j, :, HD:]
                o_ref[:, j * HD:(j + 1) * HD] = (acc_scr[j, :, :HD] / total).astype(o_ref.dtype)
            else:
                o_ref[:, j * HD:(j + 1) * HD] = (acc_scr[j] / l_scr[j]).astype(o_ref.dtype)


def attend(nback, full, queries, keys, values, qids, kids, half, halves, mxu_sum=MXU_SUM):
    rows, width = queries.shape
    width = width // halves
    heads = width // HD
    n_q = rows // BLOCK
    base = keys.shape[0] // BLOCK - n_q
    n_steps = DOC_BLOCKS + 1

    def kv_map(qb, step, nback_ref, full_ref):
        return (base + qb - jnp.minimum(step, nback_ref[qb]), 0)

    def kid_map(qb, step, nback_ref, full_ref):
        return (0, base + qb - jnp.minimum(step, nback_ref[qb]))

    grid_spec = pltpu.PrefetchScalarGridSpec(
        num_scalar_prefetch=2,
        grid=(n_q, n_steps),
        in_specs=[
            pl.BlockSpec((BLOCK, width), lambda qb, step, nb, fl: (qb, half)),
            pl.BlockSpec((BLOCK, HD), kv_map),
            pl.BlockSpec((BLOCK, HD), kv_map),
            pl.BlockSpec((BLOCK, 1), lambda qb, step, nb, fl: (qb, 0)),
            pl.BlockSpec((1, BLOCK), kid_map),
        ],
        out_specs=pl.BlockSpec((BLOCK, width), lambda qb, step, nb, fl: (qb, 0)),
        scratch_shapes=[
            pltpu.VMEM((heads, BLOCK, 128), jnp.float32),
            pltpu.VMEM((heads, BLOCK, 128), jnp.float32),
            pltpu.VMEM((heads, BLOCK, 2 * HD if mxu_sum else HD), jnp.float32),
        ],
    )
    flops = 40 * rows * keys.shape[0] // 2 * HD * heads
    return pl.pallas_call(
        functools.partial(attend_kernel, heads=heads, n_steps=n_steps, mxu_sum=mxu_sum),
        out_shape=jax.ShapeDtypeStruct((rows, width), queries.dtype),
        grid_spec=grid_spec,
        compiler_params=pltpu.CompilerParams(dimension_semantics=("arbitrary", "arbitrary")),
        cost_estimate=pl.CostEstimate(
            flops=flops, transcendentals=flops // (20 * HD), bytes_accessed=4 * rows * width),
    )(nback, full, queries, keys, values, qids, kids)


def shards(queries, keys, values, doc_ids):
    range_rows = QBLK_DEV * BLOCK
    rows = queries.shape[0]
    heads_axis = lax.axis_size("head")
    ctx_pos = lax.axis_index("ctx")
    paired = jnp.concatenate(
        [keys.reshape(rows, heads_axis, -1), values.reshape(rows, heads_axis, -1)], axis=2)
    local_pair = lax.all_to_all(paired, "head", split_axis=1, concat_axis=0, tiled=True)
    local_queries = lax.all_to_all(queries, "head", split_axis=1, concat_axis=0, tiled=True)
    local_pair = local_pair.reshape(range_rows, 2 * HD)
    prev1 = from_behind(local_pair, "ctx", 1)
    prev2 = from_behind(local_pair[range_rows - BLOCK:], "ctx", 2)
    window = jnp.concatenate([prev2, prev1, local_pair], axis=0)
    reach = BLOCK + range_rows
    n_q = range_rows // BLOCK
    n_steps = DOC_BLOCKS + 1
    base = reach // BLOCK
    window_start = ctx_pos * range_rows - reach
    positions = window_start + jnp.arange(reach + range_rows, dtype=jnp.int32)
    window_ids = lax.dynamic_slice_in_dim(doc_ids, jnp.maximum(window_start, 0), reach + range_rows)
    shift = jnp.minimum(window_start, 0)
    window_ids = jnp.where(positions < 0, -1, jnp.roll(window_ids, -shift))
    range_ids = window_ids[reach:]
    tile_first = window_ids.reshape(-1, BLOCK)[:, 0]
    tile_last = window_ids.reshape(-1, BLOCK)[:, BLOCK - 1]
    first_q = range_ids.reshape(-1, BLOCK)[:, 0]
    last_q = range_ids.reshape(-1, BLOCK)[:, BLOCK - 1]
    steps = np.arange(n_steps)
    tiles = base + np.arange(n_q)[:, None] - steps[None, :]
    live = (tile_last[tiles] == first_q[:, None]) & (steps[None, :] > 0)
    nback = jnp.sum(live.astype(jnp.int32), axis=1)
    full = ((tile_first[tiles] == last_q[:, None]) & (steps[None, :] > 0)).astype(jnp.int32).reshape(-1)
    window_keys, window_values = window[:, :HD], window[:, HD:]
    qids, kids = range_ids.reshape(range_rows, 1), window_ids.reshape(1, -1)
    outs = []
    for half in range(SPLIT):
        local_out = attend(nback, full, local_queries, window_keys, window_values, qids, kids, half, SPLIT)
        outs.append(lax.all_to_all(
            local_out.reshape(range_rows, 1, -1), "head", split_axis=0, concat_axis=1, tiled=True))
    return jnp.stack(outs, axis=2).reshape(rows, QH * HD)


def solution(mesh):
    in_specs = (P(("ctx", "head"), None), P(("ctx", "head"), None), P(("ctx", "head"), None), P())
    out_specs = P(("ctx", "head"), None)
    return jax.shard_map(shards, mesh=mesh, in_specs=in_specs, out_specs=out_specs, check_vma=False)
```

```python
import functools

import numpy as np

import jax
import jax.numpy as jnp
from jax import lax
from jax.experimental import pallas as pl
from jax.experimental.pallas import tpu as pltpu
from jax.sharding import PartitionSpec as P

HD = 128
QH = 64
KVH = 8
BLOCK = 256
DOC_BLOCKS = 5
QBLK_DEV = 4
PREV = 2
MXU_SUM = True


floor_score = -1e30


def from_behind(value, axis, steps):
    count = lax.axis_size(axis)
    leading, last = (max(0, -steps), min(count, count - steps))
    return lax.ppermute(value, axis, [(source, source + steps) for source in range(leading, last)])


def key_window(paired):
    pieces = []
    for offset in range(1, PREV + 1):
        pieces.append(from_behind(paired, "ctx", offset))
    return jnp.concatenate(pieces[::-1] + [paired], axis=1)


def attend_kernel(nback_ref, full_ref, q_ref, k_ref, v_ref, qid_ref, kid_ref, o_ref, m_scr, l_scr, acc_scr, *, heads, n_steps, mxu_sum):
    qb = pl.program_id(0)
    step = pl.program_id(1)
    last = pl.num_programs(1) - 1
    half = BLOCK // 2

    def augmented(v):
        return jnp.concatenate([v, jnp.ones_like(v)], axis=1)

    @pl.when(step == 0)
    def _diagonal():
        k = k_ref[...]
        v = augmented(v_ref[...])
        same = qid_ref[...] == kid_ref[...]
        rows = lax.broadcasted_iota(jnp.int32, (BLOCK, BLOCK), 0)
        cols = lax.broadcasted_iota(jnp.int32, (BLOCK, BLOCK), 1)
        allowed = same & (cols <= rows)
        for j in range(heads):
            q = q_ref[:, j * HD:(j + 1) * HD]
            for lo, width in ((0, half), (half, BLOCK)):
                s = lax.dot_general(q[lo:lo + half], k[:width], (((1,), (1,)), ((), ())),
                                    preferred_element_type=jnp.float32)
                s = s * HD ** (-0.5)
                s = jnp.where(allowed[lo:lo + half, :width], s, floor_score)
                m_new = jnp.max(s, axis=-1, keepdims=True)
                p = jnp.exp(s - m_new)
                acc_scr[j, lo:lo + half] = jnp.dot(
                    p.astype(jnp.bfloat16), v[:width], preferred_element_type=jnp.float32)
                m_scr[j, lo:lo + half] = jnp.broadcast_to(m_new, (half, 128))

    def body(masked):
        k = k_ref[...]
        v = augmented(v_ref[...])
        if masked:
            allowed = qid_ref[...] == kid_ref[...]
        for j in range(heads):
            q = q_ref[:, j * HD:(j + 1) * HD]
            s = lax.dot_general(q, k, (((1,), (1,)), ((), ())), preferred_element_type=jnp.float32)
            s = s * HD ** (-0.5)
            if masked:
                s = jnp.where(allowed, s, floor_score)
            m_old = m_scr[j]
            m_new = jnp.maximum(m_old, jnp.max(s, axis=-1, keepdims=True))
            factor = jnp.exp(m_old - m_new)
            p = jnp.exp(s - jnp.tile(m_new, (1, BLOCK // 128)))
            pv = jnp.dot(p.astype(jnp.bfloat16), v, preferred_element_type=jnp.float32)
            acc_scr[j] = acc_scr[j] * jnp.tile(factor, (1, 2)) + pv
            m_scr[j] = m_new

    live = (step > 0) & (step <= nback_ref[qb])
    full = full_ref[qb * n_steps + step] > 0

    @pl.when(live & full)
    def _plain():
        body(False)

    @pl.when(live & jnp.logical_not(full))
    def _masked():
        body(True)

    @pl.when(step == last)
    def _finish():
        for j in range(heads):
            total = acc_scr[j, :, HD:]
            o_ref[:, j * HD:(j + 1) * HD] = (acc_scr[j, :, :HD] / total).astype(o_ref.dtype)


def attend(nback, full, queries, keys, values, qids, kids, mxu_sum=MXU_SUM):
    rows, width = queries.shape
    heads = width // HD
    n_q = rows // BLOCK
    base = keys.shape[0] // BLOCK - n_q
    n_steps = DOC_BLOCKS + 1

    def kv_map(qb, step, nback_ref, full_ref):
        return (base + qb - jnp.minimum(step, nback_ref[qb]), 0)

    def kid_map(qb, step, nback_ref, full_ref):
        return (0, base + qb - jnp.minimum(step, nback_ref[qb]))

    grid_spec = pltpu.PrefetchScalarGridSpec(
        num_scalar_prefetch=2,
        grid=(n_q, n_steps),
        in_specs=[
            pl.BlockSpec((BLOCK, width), lambda qb, step, nb, fl: (qb, 0)),
            pl.BlockSpec((BLOCK, HD), kv_map),
            pl.BlockSpec((BLOCK, HD), kv_map),
            pl.BlockSpec((BLOCK, 1), lambda qb, step, nb, fl: (qb, 0)),
            pl.BlockSpec((1, BLOCK), kid_map),
        ],
        out_specs=pl.BlockSpec((BLOCK, width), lambda qb, step, nb, fl: (qb, 0)),
        scratch_shapes=[
            pltpu.VMEM((heads, BLOCK, 128), jnp.float32),
            pltpu.VMEM((heads, BLOCK, 128), jnp.float32),
            pltpu.VMEM((heads, BLOCK, 2 * HD if mxu_sum else HD), jnp.float32),
        ],
    )
    flops = 40 * rows * keys.shape[0] // 2 * HD * heads
    return pl.pallas_call(
        functools.partial(attend_kernel, heads=heads, n_steps=n_steps, mxu_sum=mxu_sum),
        out_shape=jax.ShapeDtypeStruct((rows, width), queries.dtype),
        grid_spec=grid_spec,
        compiler_params=pltpu.CompilerParams(dimension_semantics=("arbitrary", "arbitrary")),
        cost_estimate=pl.CostEstimate(
            flops=flops, transcendentals=flops // (20 * HD), bytes_accessed=4 * rows * width),
    )(nback, full, queries, keys, values, qids, kids)


def shards(queries, keys, values, doc_ids):
    range_rows = QBLK_DEV * BLOCK
    rows = queries.shape[0]
    heads_axis = lax.axis_size("head")
    ctx_pos = lax.axis_index("ctx")
    paired = jnp.concatenate(
        [keys.reshape(rows, heads_axis, -1), values.reshape(rows, heads_axis, -1)], axis=2)
    local_pair = lax.all_to_all(paired, "head", split_axis=1, concat_axis=0, tiled=True)
    local_queries = lax.all_to_all(queries, "head", split_axis=1, concat_axis=0, tiled=True)
    local_pair = local_pair.reshape(range_rows, 2 * HD)
    prev1 = from_behind(local_pair, "ctx", 1)
    prev2 = from_behind(local_pair[range_rows - BLOCK:], "ctx", 2)
    window = jnp.concatenate([prev2, prev1, local_pair], axis=0)
    reach = BLOCK + range_rows
    n_q = range_rows // BLOCK
    n_steps = DOC_BLOCKS + 1
    base = reach // BLOCK
    window_start = ctx_pos * range_rows - reach
    positions = window_start + jnp.arange(reach + range_rows, dtype=jnp.int32)
    window_ids = lax.dynamic_slice_in_dim(doc_ids, jnp.maximum(window_start, 0), reach + range_rows)
    shift = jnp.minimum(window_start, 0)
    window_ids = jnp.where(positions < 0, -1, jnp.roll(window_ids, -shift))
    range_ids = window_ids[reach:]
    tile_first = window_ids.reshape(-1, BLOCK)[:, 0]
    tile_last = window_ids.reshape(-1, BLOCK)[:, BLOCK - 1]
    first_q = range_ids.reshape(-1, BLOCK)[:, 0]
    last_q = range_ids.reshape(-1, BLOCK)[:, BLOCK - 1]
    steps = np.arange(n_steps)
    tiles = base + np.arange(n_q)[:, None] - steps[None, :]
    live = (tile_last[tiles] == first_q[:, None]) & (steps[None, :] > 0)
    nback = jnp.sum(live.astype(jnp.int32), axis=1)
    full = ((tile_first[tiles] == last_q[:, None]) & (steps[None, :] > 0)).astype(jnp.int32).reshape(-1)
    local_out = attend(
        nback, full, local_queries, window[:, :HD], window[:, HD:],
        range_ids.reshape(range_rows, 1), window_ids.reshape(1, -1))
    return lax.all_to_all(local_out, "head", split_axis=0, concat_axis=1, tiled=True)


def solution(mesh):
    in_specs = (P(("ctx", "head"), None), P(("ctx", "head"), None), P(("ctx", "head"), None), P())
    out_specs = P(("ctx", "head"), None)
    return jax.shard_map(shards, mesh=mesh, in_specs=in_specs, out_specs=out_specs, check_vma=False)
```

```python
import functools

import numpy as np

import jax
import jax.numpy as jnp
from jax import lax
from jax.experimental import pallas as pl
from jax.experimental.pallas import tpu as pltpu
from jax.sharding import PartitionSpec as P

HD = 128
QH = 64
KVH = 8
BLOCK = 256
DOC_BLOCKS = 5
QBLK_DEV = 4
PREV = 2
MXU_SUM = True


floor_score = -1e30


def from_behind(value, axis, steps):
    count = lax.axis_size(axis)
    leading, last = (max(0, -steps), min(count, count - steps))
    return lax.ppermute(value, axis, [(source, source + steps) for source in range(leading, last)])


def key_window(paired):
    pieces = []
    for offset in range(1, PREV + 1):
        pieces.append(from_behind(paired, "ctx", offset))
    return jnp.concatenate(pieces[::-1] + [paired], axis=1)


def attend_kernel(nback_ref, full_ref, q_ref, k_ref, v_ref, qid_ref, kid_ref, o_ref, m_scr, l_scr, acc_scr, *, heads, n_steps, mxu_sum):
    qb = pl.program_id(0)
    step = pl.program_id(1)
    last = pl.num_programs(1) - 1
    half = BLOCK // 2

    def augmented(v):
        return jnp.concatenate([v, jnp.ones_like(v)], axis=1)

    @pl.when(step == 0)
    def _diagonal():
        k = k_ref[...]
        v = augmented(v_ref[...])
        same = qid_ref[...] == kid_ref[...]
        rows = lax.broadcasted_iota(jnp.int32, (BLOCK, BLOCK), 0)
        cols = lax.broadcasted_iota(jnp.int32, (BLOCK, BLOCK), 1)
        allowed = same & (cols <= rows)
        for j in range(heads):
            q = q_ref[:, j * HD:(j + 1) * HD]
            for lo, width in ((0, half), (half, BLOCK)):
                s = lax.dot_general(q[lo:lo + half], k[:width], (((1,), (1,)), ((), ())),
                                    preferred_element_type=jnp.float32)
                s = s * HD ** (-0.5)
                s = jnp.where(allowed[lo:lo + half, :width], s, floor_score)
                m_new = jnp.max(s, axis=-1, keepdims=True)
                p = jnp.exp(s - m_new)
                acc_scr[j, lo:lo + half] = jnp.dot(
                    p.astype(jnp.bfloat16), v[:width], preferred_element_type=jnp.float32)
                m_scr[j, lo:lo + half] = jnp.broadcast_to(m_new, (half, 128))

    def body(masked):
        k = k_ref[...]
        v = augmented(v_ref[...])
        if masked:
            allowed = qid_ref[...] == kid_ref[...]
        for j in range(heads):
            q = q_ref[:, j * HD:(j + 1) * HD]
            s = lax.dot_general(q, k, (((1,), (1,)), ((), ())), preferred_element_type=jnp.float32)
            s = s * HD ** (-0.5)
            if masked:
                s = jnp.where(allowed, s, floor_score)
            m_old = m_scr[j]
            m_new = jnp.maximum(m_old, jnp.max(s, axis=-1, keepdims=True))
            factor = jnp.exp(m_old - m_new)
            p = jnp.exp(s - jnp.tile(m_new, (1, BLOCK // 128)))
            pv = jnp.dot(p.astype(jnp.bfloat16), v, preferred_element_type=jnp.float32)
            acc_scr[j] = acc_scr[j] * jnp.tile(factor, (1, 2)) + pv
            m_scr[j] = m_new

    live = (step > 0) & (step <= nback_ref[qb])
    full = full_ref[qb * n_steps + step] > 0

    @pl.when(live & full)
    def _plain():
        body(False)

    @pl.when(live & jnp.logical_not(full))
    def _masked():
        body(True)

    @pl.when(step == last)
    def _finish():
        for j in range(heads):
            total = acc_scr[j, :, HD:]
            o_ref[:, j * HD:(j + 1) * HD] = (acc_scr[j, :, :HD] / total).astype(o_ref.dtype)


def attend(nback, full, queries, keys, values, qids, kids, mxu_sum=MXU_SUM):
    rows, width = queries.shape
    heads = width // HD
    n_q = rows // BLOCK
    base = keys.shape[0] // BLOCK - n_q
    n_steps = DOC_BLOCKS + 1

    def kv_map(qb, step, nback_ref, full_ref):
        return (base + qb - jnp.minimum(step, nback_ref[qb]), 0)

    def kid_map(qb, step, nback_ref, full_ref):
        return (0, base + qb - jnp.minimum(step, nback_ref[qb]))

    grid_spec = pltpu.PrefetchScalarGridSpec(
        num_scalar_prefetch=2,
        grid=(n_q, n_steps),
        in_specs=[
            pl.BlockSpec((BLOCK, width), lambda qb, step, nb, fl: (qb, 0)),
            pl.BlockSpec((BLOCK, HD), kv_map),
            pl.BlockSpec((BLOCK, HD), kv_map),
            pl.BlockSpec((BLOCK, 1), lambda qb, step, nb, fl: (qb, 0)),
            pl.BlockSpec((1, BLOCK), kid_map),
        ],
        out_specs=pl.BlockSpec((BLOCK, width), lambda qb, step, nb, fl: (qb, 0)),
        scratch_shapes=[
            pltpu.VMEM((heads, BLOCK, 128), jnp.float32),
            pltpu.VMEM((heads, BLOCK, 128), jnp.float32),
            pltpu.VMEM((heads, BLOCK, 2 * HD if mxu_sum else HD), jnp.float32),
        ],
    )
    flops = 40 * rows * keys.shape[0] // 2 * HD * heads
    return pl.pallas_call(
        functools.partial(attend_kernel, heads=heads, n_steps=n_steps, mxu_sum=mxu_sum),
        out_shape=jax.ShapeDtypeStruct((rows, width), queries.dtype),
        grid_spec=grid_spec,
        compiler_params=pltpu.CompilerParams(dimension_semantics=("arbitrary", "arbitrary")),
        cost_estimate=pl.CostEstimate(
            flops=flops, transcendentals=flops // (20 * HD), bytes_accessed=4 * rows * width),
    )(nback, full, queries, keys, values, qids, kids)


def shards(queries, keys, values, doc_ids):
    range_rows = QBLK_DEV * BLOCK
    rows = queries.shape[0]
    heads_axis = lax.axis_size("head")
    ctx_pos = lax.axis_index("ctx")
    paired = jnp.concatenate(
        [keys.reshape(rows, heads_axis, -1), values.reshape(rows, heads_axis, -1)], axis=2)
    local_pair = lax.all_to_all(paired, "head", split_axis=1, concat_axis=0, tiled=True)
    local_pair = local_pair.reshape(range_rows, 2 * HD)
    prev1 = from_behind(local_pair, "ctx", 1)
    prev2 = from_behind(local_pair[range_rows - BLOCK:], "ctx", 2)
    queries, prev1, prev2 = lax.optimization_barrier((queries, prev1, prev2))
    local_queries = lax.all_to_all(queries, "head", split_axis=1, concat_axis=0, tiled=True)
    window = jnp.concatenate([prev2, prev1, local_pair], axis=0)
    reach = BLOCK + range_rows
    n_q = range_rows // BLOCK
    n_steps = DOC_BLOCKS + 1
    base = reach // BLOCK
    window_start = ctx_pos * range_rows - reach
    positions = window_start + jnp.arange(reach + range_rows, dtype=jnp.int32)
    window_ids = lax.dynamic_slice_in_dim(doc_ids, jnp.maximum(window_start, 0), reach + range_rows)
    shift = jnp.minimum(window_start, 0)
    window_ids = jnp.where(positions < 0, -1, jnp.roll(window_ids, -shift))
    range_ids = window_ids[reach:]
    tile_first = window_ids.reshape(-1, BLOCK)[:, 0]
    tile_last = window_ids.reshape(-1, BLOCK)[:, BLOCK - 1]
    first_q = range_ids.reshape(-1, BLOCK)[:, 0]
    last_q = range_ids.reshape(-1, BLOCK)[:, BLOCK - 1]
    steps = np.arange(n_steps)
    tiles = base + np.arange(n_q)[:, None] - steps[None, :]
    live = (tile_last[tiles] == first_q[:, None]) & (steps[None, :] > 0)
    nback = jnp.sum(live.astype(jnp.int32), axis=1)
    full = ((tile_first[tiles] == last_q[:, None]) & (steps[None, :] > 0)).astype(jnp.int32).reshape(-1)
    local_out = attend(
        nback, full, local_queries, window[:, :HD], window[:, HD:],
        range_ids.reshape(range_rows, 1), window_ids.reshape(1, -1))
    return lax.all_to_all(local_out, "head", split_axis=0, concat_axis=1, tiled=True)


def solution(mesh):
    in_specs = (P(("ctx", "head"), None), P(("ctx", "head"), None), P(("ctx", "head"), None), P())
    out_specs = P(("ctx", "head"), None)
    return jax.shard_map(shards, mesh=mesh, in_specs=in_specs, out_specs=out_specs, check_vma=False)
```

```python
import functools

import numpy as np

import jax
import jax.numpy as jnp
from jax import lax
from jax.experimental import pallas as pl
from jax.experimental.pallas import tpu as pltpu
from jax.sharding import PartitionSpec as P

HD = 128
QH = 64
KVH = 8
BLOCK = 256
DOC_BLOCKS = 5
QBLK_DEV = 4
PREV = 2
MXU_SUM = True


floor_score = -1e30


def from_behind(value, axis, steps):
    count = lax.axis_size(axis)
    leading, last = (max(0, -steps), min(count, count - steps))
    return lax.ppermute(value, axis, [(source, source + steps) for source in range(leading, last)])


def key_window(paired):
    pieces = []
    for offset in range(1, PREV + 1):
        pieces.append(from_behind(paired, "ctx", offset))
    return jnp.concatenate(pieces[::-1] + [paired], axis=1)


def attend_kernel(nback_ref, full_ref, q_ref, k_ref, v_ref, qid_ref, kid_ref, o_ref, m_scr, acc_scr, *, heads, n_steps, base):
    qb = pl.program_id(0)
    diag = base + qb

    def visit(tile, masked, causal):
        start = pl.multiple_of(tile * BLOCK, BLOCK)
        k = k_ref[pl.ds(start, BLOCK), :]
        v = v_ref[pl.ds(start, BLOCK), :]
        v = jnp.concatenate([v, jnp.ones_like(v)], axis=1)
        if masked:
            allowed = qid_ref[...] == kid_ref[:, pl.ds(start, BLOCK)]
            if causal:
                rows = lax.broadcasted_iota(jnp.int32, (BLOCK, BLOCK), 0)
                cols = lax.broadcasted_iota(jnp.int32, (BLOCK, BLOCK), 1)
                allowed = allowed & (cols <= rows)
        for j in range(heads):
            q = q_ref[:, j * HD:(j + 1) * HD]
            s = lax.dot_general(q, k, (((1,), (1,)), ((), ())), preferred_element_type=jnp.float32)
            s = s * HD ** (-0.5)
            if masked:
                s = jnp.where(allowed, s, floor_score)
            m_old = m_scr[j]
            m_new = jnp.maximum(m_old, jnp.max(s, axis=-1, keepdims=True))
            factor = jnp.exp(m_old - m_new)
            p = jnp.exp(s - jnp.tile(m_new, (1, BLOCK // 128)))
            pv = jnp.dot(p.astype(jnp.bfloat16), v, preferred_element_type=jnp.float32)
            acc_scr[j] = acc_scr[j] * jnp.tile(factor, (1, 2)) + pv
            m_scr[j] = m_new

    m_scr[...] = jnp.full(m_scr.shape, floor_score, jnp.float32)
    acc_scr[...] = jnp.zeros(acc_scr.shape, jnp.float32)
    visit(diag, True, True)

    def back(step, carry):
        tile = diag - step
        full = full_ref[qb * n_steps + step] > 0

        @pl.when(full)
        def _plain():
            visit(tile, False, False)

        @pl.when(jnp.logical_not(full))
        def _masked():
            visit(tile, True, False)

        return carry

    lax.fori_loop(1, nback_ref[qb] + 1, back, 0)
    for j in range(heads):
        total = acc_scr[j, :, HD:]
        o_ref[:, j * HD:(j + 1) * HD] = (acc_scr[j, :, :HD] / total).astype(o_ref.dtype)


def attend(nback, full, queries, keys, values, qids, kids):
    rows, width = queries.shape
    heads = width // HD
    n_q = rows // BLOCK
    span = keys.shape[0]
    base = span // BLOCK - n_q
    n_steps = DOC_BLOCKS + 1

    whole = lambda qb, nb, fl: (0, 0)
    grid_spec = pltpu.PrefetchScalarGridSpec(
        num_scalar_prefetch=2,
        grid=(n_q,),
        in_specs=[
            pl.BlockSpec((BLOCK, width), lambda qb, nb, fl: (qb, 0)),
            pl.BlockSpec((span, HD), whole),
            pl.BlockSpec((span, HD), whole),
            pl.BlockSpec((BLOCK, 1), lambda qb, nb, fl: (qb, 0)),
            pl.BlockSpec((1, span), whole),
        ],
        out_specs=pl.BlockSpec((BLOCK, width), lambda qb, nb, fl: (qb, 0)),
        scratch_shapes=[
            pltpu.VMEM((heads, BLOCK, 128), jnp.float32),
            pltpu.VMEM((heads, BLOCK, 2 * HD), jnp.float32),
        ],
    )
    flops = 40 * rows * span // 2 * HD * heads
    return pl.pallas_call(
        functools.partial(attend_kernel, heads=heads, n_steps=n_steps, base=base),
        out_shape=jax.ShapeDtypeStruct((rows, width), queries.dtype),
        grid_spec=grid_spec,
        compiler_params=pltpu.CompilerParams(dimension_semantics=("arbitrary",)),
        cost_estimate=pl.CostEstimate(
            flops=flops, transcendentals=flops // (20 * HD), bytes_accessed=4 * rows * width),
    )(nback, full, queries, keys, values, qids, kids)


def shards(queries, keys, values, doc_ids):
    range_rows = QBLK_DEV * BLOCK
    rows = queries.shape[0]
    heads_axis = lax.axis_size("head")
    ctx_pos = lax.axis_index("ctx")
    paired = jnp.concatenate(
        [keys.reshape(rows, heads_axis, -1), values.reshape(rows, heads_axis, -1)], axis=2)
    local_pair = lax.all_to_all(paired, "head", split_axis=1, concat_axis=0, tiled=True)
    local_queries = lax.all_to_all(queries, "head", split_axis=1, concat_axis=0, tiled=True)
    local_pair = local_pair.reshape(range_rows, 2 * HD)
    prev1 = from_behind(local_pair, "ctx", 1)
    prev2 = from_behind(local_pair[range_rows - BLOCK:], "ctx", 2)
    window = jnp.concatenate([prev2, prev1, local_pair], axis=0)
    reach = BLOCK + range_rows
    n_q = range_rows // BLOCK
    n_steps = DOC_BLOCKS + 1
    base = reach // BLOCK
    window_start = ctx_pos * range_rows - reach
    positions = window_start + jnp.arange(reach + range_rows, dtype=jnp.int32)
    window_ids = lax.dynamic_slice_in_dim(doc_ids, jnp.maximum(window_start, 0), reach + range_rows)
    shift = jnp.minimum(window_start, 0)
    window_ids = jnp.where(positions < 0, -1, jnp.roll(window_ids, -shift))
    range_ids = window_ids[reach:]
    tile_first = window_ids.reshape(-1, BLOCK)[:, 0]
    tile_last = window_ids.reshape(-1, BLOCK)[:, BLOCK - 1]
    first_q = range_ids.reshape(-1, BLOCK)[:, 0]
    last_q = range_ids.reshape(-1, BLOCK)[:, BLOCK - 1]
    steps = np.arange(n_steps)
    tiles = base + np.arange(n_q)[:, None] - steps[None, :]
    live = (tile_last[tiles] == first_q[:, None]) & (steps[None, :] > 0)
    nback = jnp.sum(live.astype(jnp.int32), axis=1)
    full = ((tile_first[tiles] == last_q[:, None]) & (steps[None, :] > 0)).astype(jnp.int32).reshape(-1)
    local_out = attend(
        nback, full, local_queries, window[:, :HD], window[:, HD:],
        range_ids.reshape(range_rows, 1), window_ids.reshape(1, -1))
    return lax.all_to_all(local_out, "head", split_axis=0, concat_axis=1, tiled=True)


def solution(mesh):
    in_specs = (P(("ctx", "head"), None), P(("ctx", "head"), None), P(("ctx", "head"), None), P())
    out_specs = P(("ctx", "head"), None)
    return jax.shard_map(shards, mesh=mesh, in_specs=in_specs, out_specs=out_specs, check_vma=False)
```
